256 devices in a mesh: ctx: 64 (over y_lo, z, x), fsdp: 4 (over y_hi, core).
Axes of the slice: x: 4, y: 4 (y_hi: 2, y_lo: 2; y = y_hi * 2 + y_lo), z: 8, core: 2. Of those that a mesh axis runs over, the one named last changes fastest.
Arguments:
- query: bfloat16 [16384, 2048], P('ctx', 'fsdp'), may hold values from -11 to 11
- key: bfloat16 [16384, 2048], P('ctx', 'fsdp'), may hold values from -11 to 11
- value: bfloat16 [16384, 2048], P('ctx', 'fsdp'), may hold values from -6 to 6
- doc_ids: int32 [16384], P('ctx'), may hold values from 0 to 19, never falling along the last dimension, each value on 1 to 2048 neighbouring positions
- out_weight: bfloat16 [2048, 4096], P(('fsdp', 'ctx')), may hold values from -0.125 to 0.125
- grad_out: bfloat16 [16384, 4096], P('ctx', 'fsdp'), may hold values from -6 to 6
Outputs:
- grad_query: bfloat16 [16384, 2048], P('ctx', 'fsdp')
- grad_key: bfloat16 [16384, 2048], P('ctx', 'fsdp')
- grad_value: bfloat16 [16384, 2048], P('ctx', 'fsdp')
- grad_out_weight: float32 [2048, 4096], P(('fsdp', 'ctx'))
The draws below stay inside these ranges and needn't reach their ends.
Inputs may be any that keep to these rules, and one draw needn't show every extreme that they name: `doc_ids`: document ids never fall along the sequence; every document has 1 to 2048 tokens and one has exactly 2048.
All inputs are finite; a program needn't handle non-finite values.
Results may differ from the reference program's by a relative error of at most 0.034.
Values may be sent and summed in bfloat16 or wider, within the bound.
No kernel may reach another device: no remote copies, remote signals or barrier semaphores. Data moves between devices by JAX's collectives and lax.ppermute only.
A program may use at most 128 MiB of HBM per device.

```python
import math
import jax
import jax.numpy as jnp
import numpy as np
from jax import lax

D = 4096
HEADS = 16
DH = 128
DOC_MOST = 2048
DOCS = 20
SEQ = 16384


def draw_query(key, part):
    drawn = jnp.clip(jax.random.normal(jax.random.fold_in(key, 101), (SEQ, HEADS * DH), jnp.float32), -6.0, 6.0)
    return drawn.astype(jnp.bfloat16)


def draw_key(key, part):
    drawn = jnp.clip(jax.random.normal(jax.random.fold_in(key, 202), (SEQ, HEADS * DH), jnp.float32), -6.0, 6.0)
    return drawn.astype(jnp.bfloat16)


def shard_levels(rng, shape, shards, smallest, largest):
    level = 1.0
    for axis_at, blocks in shards:
        draws = jax.random.uniform(jax.random.fold_in(jax.random.fold_in(rng, 6), axis_at), (blocks,), jnp.float32, smallest / len(shards), largest / len(shards))
        level = level * jnp.repeat(jnp.exp(draws), shape[axis_at] // blocks).reshape((-1,) + (1,) * (len(shape) - 1 - axis_at))
    return level


def profile(number_of, total, reach, slope):
    weights = [(1 << 20) // math.isqrt(grade ** slope) + 1 for grade in range(2, number_of + 1)]
    rest, given = total - reach - (number_of - 1), [1] * (number_of - 1)
    while rest > 0:
        movable = [i for i in range(number_of - 1) if given[i] < reach]
        whole, budget = sum([weights[i] for i in movable]), rest
        for i in movable:
            more = min(reach - given[i], max(1, budget * weights[i] // whole), rest)
            given[i] = given[i] + more
            rest = rest - more
    return np.array([reach] + given)


def ragged_sizes(own_key, count, total, limit, skew):
    if count == 2:
        one = jax.random.randint(own_key, (), max(1, total - limit), min(limit, total - 1) + 1)
        return jnp.stack([one, total - one])
    lengths = jnp.asarray(profile(count, total, limit, skew), jnp.int32)
    couples = (count - 1) // 2
    source_of, taker = lengths[1:1 + 2 * couples:2], lengths[2:2 + 2 * couples:2]
    slack = jnp.minimum(source_of - 1, limit - taker)
    passed = jax.random.randint(jax.random.fold_in(own_key, 1), (couples,), 0, 1 << 20) % (slack + 1)
    lengths = lengths.at[1:1 + 2 * couples:2].set(source_of - passed).at[2:2 + 2 * couples:2].set(taker + passed)
    return lengths[jax.random.permutation(jax.random.fold_in(own_key, 2), count)]


def normal_values(key, shape, spread, limit, split=(), kind=jnp.bfloat16):
    values = jax.random.normal(key, shape, jnp.float32) * spread
    if len(split) > 0:
        values = shard_levels(key, shape, split, -0.22, 0.18) * values
    return jnp.clip(values, min=-limit, max=limit).astype(kind)


def setup_inputs(seed: int = 0) -> dict:
    key_list = jax.random.split(jax.random.key(seed), 7)
    return {
        "query": draw_query(jax.random.fold_in(key_list[6], 71), 0),
        "key": draw_key(jax.random.fold_in(key_list[6], 71), 0),
        "value": normal_values(key_list[2], (SEQ, HEADS * DH), 1.0, 6.0, ((0, 64), (1, 4))),
        "doc_ids": jnp.searchsorted(jnp.cumsum(ragged_sizes(key_list[3], DOCS, SEQ, DOC_MOST, 2)), jnp.arange(SEQ), side="right").astype(jnp.int32),
        "out_weight": normal_values(key_list[4], (HEADS * DH, D), (HEADS * DH) ** -0.5, 0.125, ((0, 256),)),
        "grad_out": normal_values(key_list[5], (SEQ, D), 1.0, 6.0, ((0, 64), (1, 4))),
    }


PRECISE = lax.Precision.HIGHEST
NEGATIVE = -1e+30

def head_major(array):
    return array.reshape(SEQ, HEADS, DH).transpose(1, 0, 2)

def reference(query, key, value, doc_ids, out_weight, grad_out):
    score_scale = 1.0 / math.sqrt(DH)
    block_rows = min(512, SEQ)
    block_count = SEQ // block_rows
    window_rows = DOC_MOST + block_rows
    token_docs = doc_ids.astype(jnp.int32)
    token_pos = jnp.arange(SEQ, dtype=jnp.int32)
    pad_docs = jnp.concatenate([jnp.full((DOC_MOST,), -1, jnp.int32), token_docs])
    pad_pos = jnp.arange(-DOC_MOST, SEQ, dtype=jnp.int32)

    def padded(array):
        return jnp.concatenate([jnp.zeros((HEADS, DOC_MOST, DH), array.dtype), array], axis=1)
    query_heads = head_major(query)
    key_pad = padded(head_major(key))
    value_pad = padded(head_major(value))

    def window(block_index, head_query, head_key):
        first_row = (block_index * block_rows).astype(jnp.int32)
        query_block = lax.dynamic_slice_in_dim(head_query, first_row, block_rows, 0)
        key_window = lax.dynamic_slice_in_dim(head_key, first_row, window_rows, 0)
        query_docs = lax.dynamic_slice_in_dim(token_docs, first_row, block_rows, 0)
        key_docs = lax.dynamic_slice_in_dim(pad_docs, first_row, window_rows, 0)
        query_pos = lax.dynamic_slice_in_dim(token_pos, first_row, block_rows, 0)
        key_pos = lax.dynamic_slice_in_dim(pad_pos, first_row, window_rows, 0)
        pair_mask = (query_docs[:, None] == key_docs[None, :]) & (key_pos[None, :] <= query_pos[:, None])
        scores = jnp.einsum('td,sd->ts', query_block.astype(jnp.float32), key_window.astype(jnp.float32), precision=PRECISE) * score_scale
        return (first_row, query_block, key_window, pair_mask, scores)

    def forward_head(head_index):
        head_query = query_heads[head_index]
        head_key = key_pad[head_index]
        head_value = value_pad[head_index]

        def one_block(block_index):
            first_row, query_block, key_window, pair_mask, scores = window(block_index, head_query, head_key)
            masked = jnp.where(pair_mask, scores, NEGATIVE)
            row_max = lax.optimization_barrier(jnp.max(masked, axis=-1))
            shifted = jnp.where(pair_mask, jnp.exp(masked - row_max[:, None]), 0.0)
            row_sum = lax.optimization_barrier(jnp.sum(shifted, axis=-1))
            log_total = row_max + jnp.log(row_sum)
            rounded = lax.optimization_barrier(shifted.astype(jnp.bfloat16)).astype(jnp.float32)
            value_window = lax.dynamic_slice_in_dim(head_value, first_row, window_rows, 0)
            output = jnp.einsum('ts,sd->td', rounded, value_window.astype(jnp.float32), precision=PRECISE) / row_sum[:, None]
            return (output, log_total)
        outputs, totals = lax.map(one_block, jnp.arange(block_count, dtype=jnp.int32))
        return (outputs.reshape(SEQ, DH), totals.reshape(SEQ))
    heads_out, heads_lse = lax.map(forward_head, jnp.arange(HEADS, dtype=jnp.int32))
    attn_heads = heads_out.astype(jnp.bfloat16)
    attention = attn_heads.transpose(1, 0, 2).reshape(SEQ, HEADS * DH)
    grad_attn = jnp.dot(grad_out, out_weight.T, preferred_element_type=jnp.float32).astype(jnp.bfloat16)
    grad_weight = jnp.dot(attention.T, grad_out, preferred_element_type=jnp.float32)
    grad_heads = head_major(grad_attn)
    delta_all = lax.optimization_barrier(jnp.sum(grad_heads.astype(jnp.float32) * attn_heads.astype(jnp.float32), axis=-1))

    def backward_head(head_index):
        head_query = query_heads[head_index]
        head_key = key_pad[head_index]
        head_value = value_pad[head_index]
        head_grad = grad_heads[head_index]
        head_lse = heads_lse[head_index]
        head_delta = delta_all[head_index]

        def one_block(carry, block_index):
            key_acc, value_acc = carry
            first_row, query_block, key_window, pair_mask, scores = window(block_index, head_query, head_key)
            value_window = lax.dynamic_slice_in_dim(head_value, first_row, window_rows, 0)
            grad_block = lax.dynamic_slice_in_dim(head_grad, first_row, block_rows, 0).astype(jnp.float32)
            lse_block = lax.dynamic_slice_in_dim(head_lse, first_row, block_rows, 0)
            delta_block = lax.dynamic_slice_in_dim(head_delta, first_row, block_rows, 0)
            weights = jnp.where(pair_mask, jnp.exp(scores - lse_block[:, None]), 0.0)
            rounded = weights.astype(jnp.bfloat16).astype(jnp.float32)
            value_part = jnp.einsum('ts,td->sd', rounded, grad_block, precision=PRECISE)
            grad_weights = jnp.einsum('td,sd->ts', grad_block, value_window.astype(jnp.float32), precision=PRECISE)
            grad_scores = (weights * (grad_weights - delta_block[:, None])).astype(jnp.bfloat16).astype(jnp.float32)
            query_part = jnp.einsum('ts,sd->td', grad_scores, key_window.astype(jnp.float32), precision=PRECISE) * score_scale
            key_part = jnp.einsum('ts,td->sd', grad_scores, query_block.astype(jnp.float32), precision=PRECISE) * score_scale
            key_old = lax.dynamic_slice_in_dim(key_acc, first_row, window_rows, 0)
            value_old = lax.dynamic_slice_in_dim(value_acc, first_row, window_rows, 0)
            key_acc = lax.dynamic_update_slice_in_dim(key_acc, key_old + key_part, first_row, 0)
            value_acc = lax.dynamic_update_slice_in_dim(value_acc, value_old + value_part, first_row, 0)
            return ((key_acc, value_acc), query_part)
        empty = jnp.zeros((SEQ + DOC_MOST, DH), jnp.float32)
        (key_acc, value_acc), query_parts = lax.scan(one_block, (empty, empty), jnp.arange(block_count, dtype=jnp.int32))
        return (query_parts.reshape(SEQ, DH), key_acc[DOC_MOST:], value_acc[DOC_MOST:])
    grad_q, grad_k, grad_v = lax.map(backward_head, jnp.arange(HEADS, dtype=jnp.int32))

    def token_major(array):
        return array.astype(jnp.bfloat16).transpose(1, 0, 2).reshape(SEQ, HEADS * DH)
    return (token_major(grad_q), token_major(grad_k), token_major(grad_v), grad_weight)
```

```python
import math

import jax
import jax.numpy as jnp
from jax import lax
from jax.sharding import Mesh
from jax.sharding import PartitionSpec as P

DH = 128

NEGATIVE = -1e30

CTX = ("cy", "cz", "cx")
FS = ("fy", "fc")
CTX_SPLIT = (2, 8, 4)


def shifted_by(array, devices, by):
    pairs = [(i, i + by) for i in range(devices) if 0 <= i + by < devices]
    return lax.ppermute(array, CTX, pairs)


def make_shards(devices):
    def shards(query, key, value, doc_ids, out_weight, grad_out):
        tok_rows = query.shape[0]
        feature_width = query.shape[1]
        head_count = feature_width // DH
        cycle_reach = max(devices // 8, 2)
        cycle_index = lax.axis_index(CTX)
        score_scale = 1.0 / math.sqrt(DH)
        local_pos = jnp.arange(tok_rows, dtype=jnp.int32)
        own_pos = cycle_index * tok_rows + local_pos
        own_docs = doc_ids + 1
        query_heads = query.reshape(tok_rows, head_count, DH)

        grad_full = lax.all_gather(grad_out, FS, axis=1, tiled=True)
        weight_rows = out_weight
        for axis in ("cx", "cz", "cy"):
            weight_rows = lax.all_gather(weight_rows, axis, axis=0, tiled=True)

        key_value = jnp.concatenate([key, value], axis=1)
        blocks = [(key, value, own_docs)]
        for cycle_step in range(1, cycle_reach + 1):
            got = shifted_by(key_value, devices, cycle_step)
            got_docs = shifted_by(own_docs, devices, cycle_step)
            blocks.append((got[:, :feature_width], got[:, feature_width:], got_docs))

        def scores_of(query_block, key_block):
            return (
                jnp.einsum("tnd,snd->nts", query_block, key_block, preferred_element_type=jnp.float32)
                * score_scale
            )

        state = (
            jnp.full((head_count, tok_rows), NEGATIVE, jnp.float32),
            jnp.zeros((head_count, tok_rows), jnp.float32),
            jnp.zeros((head_count, tok_rows, DH), jnp.float32),
        )
        stored_blocks = []
        for cycle_step in range(cycle_reach + 1):
            key_rows, value_rows, key_docs = blocks[cycle_step]
            key_block = key_rows.reshape(tok_rows, head_count, DH)
            value_block = value_rows.reshape(tok_rows, head_count, DH)
            key_pos = own_pos - cycle_step * tok_rows
            pair_mask = (own_docs[:, None] == key_docs[None, :]) & (
                key_pos[None, :] <= own_pos[:, None]
            )
            forward_row_max, forward_row_sum, forward_output_sum = state
            forward_scores = jnp.where(pair_mask[None], scores_of(query_heads, key_block), NEGATIVE)
            new_max = jnp.maximum(forward_row_max, jnp.max(forward_scores, axis=-1))
            decay_factor = jnp.exp(forward_row_max - new_max)
            forward_weights = jnp.where(
                pair_mask[None], jnp.exp(forward_scores - new_max[..., None]), 0.0
            )
            new_sum = forward_row_sum * decay_factor + jnp.sum(forward_weights, axis=-1)
            weights_low = forward_weights.astype(jnp.bfloat16)
            new_output = forward_output_sum * decay_factor[..., None] + jnp.einsum(
                "nts,snd->ntd", weights_low, value_block, preferred_element_type=jnp.float32
            )
            state = (new_max, new_sum, new_output)
            stored_blocks.append((key_block, value_block, pair_mask))
        row_max, row_sum, output_sum = state
        log_total = row_max + jnp.log(row_sum)
        attn_heads = (output_sum / row_sum[..., None]).astype(jnp.bfloat16).transpose(1, 0, 2)
        attention = attn_heads.reshape(tok_rows, feature_width)

        partial_weight = lax.dot_general(
            attention, grad_full, (((0,), (0,)), ((), ())), preferred_element_type=jnp.float32
        )
        rows_each = partial_weight.shape[0] // devices
        partial_weight = (
            partial_weight.reshape(*CTX_SPLIT, rows_each, partial_weight.shape[1])
            .transpose(1, 2, 0, 3, 4)
            .reshape(partial_weight.shape)
        )
        for axis in ("cz", "cx", "cy"):
            partial_weight = lax.psum_scatter(partial_weight, axis, scatter_dimension=0, tiled=True)
        grad_weight = partial_weight

        grad_attn = lax.dot_general(
            grad_full,
            weight_rows,
            (((1,), (1,)), ((), ())),
            preferred_element_type=jnp.float32,
        ).astype(jnp.bfloat16)
        grad_heads = grad_attn.reshape(tok_rows, head_count, DH)
        delta_sum = jnp.einsum(
            "tnd,tnd->nt", grad_heads, attn_heads, preferred_element_type=jnp.float32
        )
        grad_query = jnp.zeros((tok_rows, head_count, DH), jnp.float32)
        grad_key = grad_value = None
        for cycle_step in range(cycle_reach + 1):
            key_block, value_block, pair_mask = stored_blocks[cycle_step]
            scores = scores_of(query_heads, key_block)
            weights = jnp.where(pair_mask[None], jnp.exp(scores - log_total[..., None]), 0.0)
            rounded = weights.astype(jnp.bfloat16)
            value_part = jnp.einsum(
                "nts,tnd->snd", rounded, grad_heads, preferred_element_type=jnp.float32
            )
            grad_weights = jnp.einsum(
                "tnd,snd->nts", grad_heads, value_block, preferred_element_type=jnp.float32
            )
            grad_scores = (weights * (grad_weights - delta_sum[..., None])).astype(jnp.bfloat16)
            query_part = (
                jnp.einsum("nts,snd->tnd", grad_scores, key_block, preferred_element_type=jnp.float32)
                * score_scale
            )
            key_part = (
                jnp.einsum("nts,tnd->snd", grad_scores, query_heads, preferred_element_type=jnp.float32)
                * score_scale
            )
            grad_query = grad_query + query_part
            key_part = key_part.reshape(tok_rows, feature_width)
            value_part = value_part.reshape(tok_rows, feature_width)
            if cycle_step == 0:
                grad_key, grad_value = key_part, value_part
            else:
                sent = jnp.concatenate([key_part, value_part], axis=1).astype(jnp.bfloat16)
                back = shifted_by(sent, devices, -cycle_step).astype(jnp.float32)
                grad_key = grad_key + back[:, :feature_width]
                grad_value = grad_value + back[:, feature_width:]
        return (
            grad_query.reshape(tok_rows, feature_width).astype(jnp.bfloat16),
            grad_key.astype(jnp.bfloat16),
            grad_value.astype(jnp.bfloat16),
            grad_weight,
        )

    return shards


def solution(mesh):
    devices = mesh.shape["ctx"]
    fine = Mesh(mesh.devices.reshape(*CTX_SPLIT, 2, mesh.shape["fsdp"] // 2), CTX + FS)
    return jax.shard_map(
        make_shards(devices),
        mesh=fine,
        in_specs=(
            P(CTX, FS),
            P(CTX, FS),
            P(CTX, FS),
            P(CTX),
            P(FS + CTX, None),
            P(CTX, FS),
        ),
        out_specs=(P(CTX, FS), P(CTX, FS), P(CTX, FS), P(FS + CTX, None)),
        check_vma=False,
    )
```

```python
import math

import jax
import jax.numpy as jnp
from jax import lax
from jax.sharding import Mesh
from jax.sharding import PartitionSpec as P

DH = 128

NEGATIVE = -1e30

CTX = ("cy", "cz", "cx")
FS = ("fy", "fc")
CTX_SPLIT = (2, 8, 4)


def shifted_by(array, devices, by):
    pairs = [(i, i + by) for i in range(devices) if 0 <= i + by < devices]
    return lax.ppermute(array, CTX, pairs)


def gathered_rows(rows, index, devices):
    bits = [devices >> k for k in (2, 3, 5, 1, 4, 6) if devices >> k >= 1]
    block = rows
    for bit in bits:
        other = lax.ppermute(block, CTX, [(i, i ^ bit) for i in range(devices)])
        low = (index & bit) == 0
        block = jnp.where(low, jnp.concatenate([block, other]), jnp.concatenate([other, block]))
    order = sorted(range(len(bits)), key=lambda k: -bits[k])
    shape = [2] * len(bits) + list(rows.shape)
    block = block.reshape(shape)
    block = block.transpose([len(bits) - 1 - k for k in order] + [len(bits), len(bits) + 1])
    return block.reshape(devices * rows.shape[0], rows.shape[1])


def make_shards(devices):
    def shards(query, key, value, doc_ids, out_weight, grad_out):
        tok_rows = query.shape[0]
        feature_width = query.shape[1]
        head_count = feature_width // DH
        cycle_reach = max(devices // 8, 2)
        cycle_index = lax.axis_index(CTX)
        score_scale = 1.0 / math.sqrt(DH)
        local_pos = jnp.arange(tok_rows, dtype=jnp.int32)
        own_pos = cycle_index * tok_rows + local_pos
        own_docs = doc_ids + 1
        query_heads = query.reshape(tok_rows, head_count, DH)

        grad_full = lax.all_gather(grad_out, FS, axis=1, tiled=True)
        weight_rows = gathered_rows(out_weight, cycle_index, devices)

        key_value = jnp.concatenate([key, value], axis=1)
        doc_row = jnp.zeros((1, 2 * feature_width), jnp.bfloat16)
        doc_row = doc_row.at[0, :tok_rows].set(own_docs.astype(jnp.bfloat16))
        key_value = jnp.concatenate([key_value, doc_row], axis=0)
        blocks = [(key, value, own_docs)]
        for cycle_step in range(1, cycle_reach + 1):
            got = shifted_by(key_value, devices, cycle_step)
            got_docs = got[tok_rows, :tok_rows].astype(jnp.int32)
            got = got[:tok_rows]
            blocks.append((got[:, :feature_width], got[:, feature_width:], got_docs))

        def scores_of(query_block, key_block):
            return (
                jnp.einsum("tnd,snd->nts", query_block, key_block, preferred_element_type=jnp.float32)
                * score_scale
            )

        state = (
            jnp.full((head_count, tok_rows), NEGATIVE, jnp.float32),
            jnp.zeros((head_count, tok_rows), jnp.float32),
            jnp.zeros((head_count, tok_rows, DH), jnp.float32),
        )
        stored_blocks = []
        for cycle_step in range(cycle_reach + 1):
            key_rows, value_rows, key_docs = blocks[cycle_step]
            key_block = key_rows.reshape(tok_rows, head_count, DH)
            value_block = value_rows.reshape(tok_rows, head_count, DH)
            key_pos = own_pos - cycle_step * tok_rows
            pair_mask = (own_docs[:, None] == key_docs[None, :]) & (
                key_pos[None, :] <= own_pos[:, None]
            )
            forward_row_max, forward_row_sum, forward_output_sum = state
            forward_scores = jnp.where(pair_mask[None], scores_of(query_heads, key_block), NEGATIVE)
            new_max = jnp.maximum(forward_row_max, jnp.max(forward_scores, axis=-1))
            decay_factor = jnp.exp(forward_row_max - new_max)
            forward_weights = jnp.where(
                pair_mask[None], jnp.exp(forward_scores - new_max[..., None]), 0.0
            )
            new_sum = forward_row_sum * decay_factor + jnp.sum(forward_weights, axis=-1)
            weights_low = forward_weights.astype(jnp.bfloat16)
            new_output = forward_output_sum * decay_factor[..., None] + jnp.einsum(
                "nts,snd->ntd", weights_low, value_block, preferred_element_type=jnp.float32
            )
            state = (new_max, new_sum, new_output)
            stored_blocks.append((key_block, value_block, pair_mask))
        row_max, row_sum, output_sum = state
        log_total = row_max + jnp.log(row_sum)
        attn_heads = (output_sum / row_sum[..., None]).astype(jnp.bfloat16).transpose(1, 0, 2)
        attention = attn_heads.reshape(tok_rows, feature_width)

        partial_weight = lax.dot_general(
            attention, grad_full, (((0,), (0,)), ((), ())), preferred_element_type=jnp.float32
        )
        rows_each = partial_weight.shape[0] // devices
        partial_weight = (
            partial_weight.reshape(*CTX_SPLIT, rows_each, partial_weight.shape[1])
            .transpose(1, 2, 0, 3, 4)
            .reshape(partial_weight.shape)
        )
        for axis in ("cz", "cx", "cy"):
            partial_weight = lax.psum_scatter(partial_weight, axis, scatter_dimension=0, tiled=True)
        grad_weight = partial_weight

        grad_attn = lax.dot_general(
            grad_full,
            weight_rows,
            (((1,), (1,)), ((), ())),
            preferred_element_type=jnp.float32,
        ).astype(jnp.bfloat16)
        grad_heads = grad_attn.reshape(tok_rows, head_count, DH)
        delta_sum = jnp.einsum(
            "tnd,tnd->nt", grad_heads, attn_heads, preferred_element_type=jnp.float32
        )
        grad_query = jnp.zeros((tok_rows, head_count, DH), jnp.float32)
        grad_key = grad_value = None
        for cycle_step in range(cycle_reach + 1):
            key_block, value_block, pair_mask = stored_blocks[cycle_step]
            scores = scores_of(query_heads, key_block)
            weights = jnp.where(pair_mask[None], jnp.exp(scores - log_total[..., None]), 0.0)
            rounded = weights.astype(jnp.bfloat16)
            value_part = jnp.einsum(
                "nts,tnd->snd", rounded, grad_heads, preferred_element_type=jnp.float32
            )
            grad_weights = jnp.einsum(
                "tnd,snd->nts", grad_heads, value_block, preferred_element_type=jnp.float32
            )
            grad_scores = (weights * (grad_weights - delta_sum[..., None])).astype(jnp.bfloat16)
            query_part = (
                jnp.einsum("nts,snd->tnd", grad_scores, key_block, preferred_element_type=jnp.float32)
                * score_scale
            )
            key_part = (
                jnp.einsum("nts,tnd->snd", grad_scores, query_heads, preferred_element_type=jnp.float32)
                * score_scale
            )
            grad_query = grad_query + query_part
            key_part = key_part.reshape(tok_rows, feature_width)
            value_part = value_part.reshape(tok_rows, feature_width)
            if cycle_step == 0:
                grad_key, grad_value = key_part, value_part
            else:
                sent = jnp.concatenate([key_part, value_part], axis=1).astype(jnp.bfloat16)
                back = shifted_by(sent, devices, -cycle_step).astype(jnp.float32)
                grad_key = grad_key + back[:, :feature_width]
                grad_value = grad_value + back[:, feature_width:]
        return (
            grad_query.reshape(tok_rows, feature_width).astype(jnp.bfloat16),
            grad_key.astype(jnp.bfloat16),
            grad_value.astype(jnp.bfloat16),
            grad_weight,
        )

    return shards


def solution(mesh):
    devices = mesh.shape["ctx"]
    fine = Mesh(mesh.devices.reshape(*CTX_SPLIT, 2, mesh.shape["fsdp"] // 2), CTX + FS)
    return jax.shard_map(
        make_shards(devices),
        mesh=fine,
        in_specs=(
            P(CTX, FS),
            P(CTX, FS),
            P(CTX, FS),
            P(CTX),
            P(FS + CTX, None),
            P(CTX, FS),
        ),
        out_specs=(P(CTX, FS), P(CTX, FS), P(CTX, FS), P(FS + CTX, None)),
        check_vma=False,
    )
```

```python
import math

import jax
import jax.numpy as jnp
from jax import lax
from jax.sharding import Mesh
from jax.sharding import PartitionSpec as P

DH = 128

NEGATIVE = -1e30

CTX = ("cy", "cz", "cx")
FS = ("fy", "fc")
CTX_SPLIT = (2, 8, 4)


def shifted_by(array, devices, by):
    pairs = [(i, i + by) for i in range(devices) if 0 <= i + by < devices]
    return lax.ppermute(array, CTX, pairs)


def gathered_rows(rows, index, devices):
    bits = [devices >> k for k in (2, 3, 5, 1, 4, 6) if devices >> k >= 1]
    block = rows
    for bit in bits:
        other = lax.ppermute(block, CTX, [(i, i ^ bit) for i in range(devices)])
        low = (index & bit) == 0
        block = jnp.where(low, jnp.concatenate([block, other]), jnp.concatenate([other, block]))
    order = sorted(range(len(bits)), key=lambda k: -bits[k])
    shape = [2] * len(bits) + list(rows.shape)
    block = block.reshape(shape)
    block = block.transpose([len(bits) - 1 - k for k in order] + [len(bits), len(bits) + 1])
    return block.reshape(devices * rows.shape[0], rows.shape[1])


def make_shards(devices):
    def shards(query, key, value, doc_ids, out_weight, grad_out):
        tok_rows = query.shape[0]
        feature_width = query.shape[1]
        head_count = feature_width // DH
        cycle_reach = max(devices // 8, 2)
        cycle_index = lax.axis_index(CTX)
        score_scale = 1.0 / math.sqrt(DH)
        local_pos = jnp.arange(tok_rows, dtype=jnp.int32)
        own_pos = cycle_index * tok_rows + local_pos
        own_docs = doc_ids + 1
        query_heads = query.reshape(tok_rows, head_count, DH)

        grad_full = lax.all_gather(grad_out, FS, axis=1, tiled=True)
        key_value = jnp.concatenate([key, value], axis=1)
        doc_row = jnp.zeros((1, 2 * feature_width), jnp.bfloat16)
        doc_row = doc_row.at[0, :tok_rows].set(own_docs.astype(jnp.bfloat16))
        key_value = jnp.concatenate([key_value, doc_row], axis=0)
        blocks = [(key, value, own_docs)]
        for cycle_step in range(1, cycle_reach + 1):
            got = shifted_by(key_value, devices, cycle_step)
            got_docs = got[tok_rows, :tok_rows].astype(jnp.int32)
            got = got[:tok_rows]
            blocks.append((got[:, :feature_width], got[:, feature_width:], got_docs))

        def scores_of(query_block, key_block):
            return (
                jnp.einsum("tnd,snd->nts", query_block, key_block, preferred_element_type=jnp.float32)
                * score_scale
            )

        state = (
            jnp.full((head_count, tok_rows), NEGATIVE, jnp.float32),
            jnp.zeros((head_count, tok_rows), jnp.float32),
            jnp.zeros((head_count, tok_rows, DH), jnp.float32),
        )
        stored_blocks = []
        for cycle_step in range(cycle_reach + 1):
            key_rows, value_rows, key_docs = blocks[cycle_step]
            key_block = key_rows.reshape(tok_rows, head_count, DH)
            value_block = value_rows.reshape(tok_rows, head_count, DH)
            key_pos = own_pos - cycle_step * tok_rows
            pair_mask = (own_docs[:, None] == key_docs[None, :]) & (
                key_pos[None, :] <= own_pos[:, None]
            )
            forward_row_max, forward_row_sum, forward_output_sum = state
            forward_scores = jnp.where(pair_mask[None], scores_of(query_heads, key_block), NEGATIVE)
            new_max = jnp.maximum(forward_row_max, jnp.max(forward_scores, axis=-1))
            decay_factor = jnp.exp(forward_row_max - new_max)
            forward_weights = jnp.where(
                pair_mask[None], jnp.exp(forward_scores - new_max[..., None]), 0.0
            )
            new_sum = forward_row_sum * decay_factor + jnp.sum(forward_weights, axis=-1)
            weights_low = forward_weights.astype(jnp.bfloat16)
            new_output = forward_output_sum * decay_factor[..., None] + jnp.einsum(
                "nts,snd->ntd", weights_low, value_block, preferred_element_type=jnp.float32
            )
            state = (new_max, new_sum, new_output)
            stored_blocks.append((key_block, value_block, pair_mask))
        row_max, row_sum, output_sum = state
        log_total = row_max + jnp.log(row_sum)
        attn_heads = (output_sum / row_sum[..., None]).astype(jnp.bfloat16).transpose(1, 0, 2)
        attention = attn_heads.reshape(tok_rows, feature_width)

        partial_weight = lax.dot_general(
            attention, grad_full, (((0,), (0,)), ((), ())), preferred_element_type=jnp.float32
        )
        rows_each = partial_weight.shape[0] // devices
        partial_weight = (
            partial_weight.reshape(*CTX_SPLIT, rows_each, partial_weight.shape[1])
            .transpose(1, 2, 0, 3, 4)
            .reshape(partial_weight.shape)
        )
        weight_local, partial_weight = lax.optimization_barrier((out_weight, partial_weight))
        for axis in ("cz", "cx", "cy"):
            partial_weight = lax.psum_scatter(partial_weight, axis, scatter_dimension=0, tiled=True)
        grad_weight = partial_weight

        weight_rows = gathered_rows(weight_local, cycle_index, devices)

        grad_attn = lax.dot_general(
            grad_full,
            weight_rows,
            (((1,), (1,)), ((), ())),
            preferred_element_type=jnp.float32,
        ).astype(jnp.bfloat16)
        grad_heads = grad_attn.reshape(tok_rows, head_count, DH)
        delta_sum = jnp.einsum(
            "tnd,tnd->nt", grad_heads, attn_heads, preferred_element_type=jnp.float32
        )
        grad_query = jnp.zeros((tok_rows, head_count, DH), jnp.float32)
        grad_key = grad_value = None
        for cycle_step in range(cycle_reach + 1):
            key_block, value_block, pair_mask = stored_blocks[cycle_step]
            scores = scores_of(query_heads, key_block)
            weights = jnp.where(pair_mask[None], jnp.exp(scores - log_total[..., None]), 0.0)
            rounded = weights.astype(jnp.bfloat16)
            value_part = jnp.einsum(
                "nts,tnd->snd", rounded, grad_heads, preferred_element_type=jnp.float32
            )
            grad_weights = jnp.einsum(
                "tnd,snd->nts", grad_heads, value_block, preferred_element_type=jnp.float32
            )
            grad_scores = (weights * (grad_weights - delta_sum[..., None])).astype(jnp.bfloat16)
            query_part = (
                jnp.einsum("nts,snd->tnd", grad_scores, key_block, preferred_element_type=jnp.float32)
                * score_scale
            )
            key_part = (
                jnp.einsum("nts,tnd->snd", grad_scores, query_heads, preferred_element_type=jnp.float32)
                * score_scale
            )
            grad_query = grad_query + query_part
            key_part = key_part.reshape(tok_rows, feature_width)
            value_part = value_part.reshape(tok_rows, feature_width)
            if cycle_step == 0:
                grad_key, grad_value = key_part, value_part
            else:
                sent = jnp.concatenate([key_part, value_part], axis=1).astype(jnp.bfloat16)
                back = shifted_by(sent, devices, -cycle_step).astype(jnp.float32)
                grad_key = grad_key + back[:, :feature_width]
                grad_value = grad_value + back[:, feature_width:]
        return (
            grad_query.reshape(tok_rows, feature_width).astype(jnp.bfloat16),
            grad_key.astype(jnp.bfloat16),
            grad_value.astype(jnp.bfloat16),
            grad_weight,
        )

    return shards


def solution(mesh):
    devices = mesh.shape["ctx"]
    fine = Mesh(mesh.devices.reshape(*CTX_SPLIT, 2, mesh.shape["fsdp"] // 2), CTX + FS)
    return jax.shard_map(
        make_shards(devices),
        mesh=fine,
        in_specs=(
            P(CTX, FS),
            P(CTX, FS),
            P(CTX, FS),
            P(CTX),
            P(FS + CTX, None),
            P(CTX, FS),
        ),
        out_specs=(P(CTX, FS), P(CTX, FS), P(CTX, FS), P(FS + CTX, None)),
        check_vma=False,
    )
```

```python
import math

import jax
import jax.numpy as jnp
from jax import lax
from jax.sharding import Mesh
from jax.sharding import PartitionSpec as P

DH = 128


NEGATIVE = -1e30

CTX = ("cy", "cz", "cx")
FS = ("fy", "fc")
CTX_SPLIT = (2, 8, 4)


def shifted_by(array, devices, by):
    pairs = [(i, i + by) for i in range(devices) if 0 <= i + by < devices]
    return lax.ppermute(array, CTX, pairs)


def gathered_rows(rows, index, devices):
    bits = [devices >> k for k in (2, 3, 5, 1, 4, 6) if devices >> k >= 1]
    block = rows
    for bit in bits:
        other = lax.ppermute(block, CTX, [(i, i ^ bit) for i in range(devices)])
        low = (index & bit) == 0
        block = jnp.where(low, jnp.concatenate([block, other]), jnp.concatenate([other, block]))
    order = sorted(range(len(bits)), key=lambda k: -bits[k])
    shape = [2] * len(bits) + list(rows.shape)
    block = block.reshape(shape)
    block = block.transpose([len(bits) - 1 - k for k in order] + [len(bits), len(bits) + 1])
    return block.reshape(devices * rows.shape[0], rows.shape[1])


def make_shards(devices):
    def shards(query, key, value, doc_ids, out_weight, grad_out):
        tok_rows = query.shape[0]
        feature_width = query.shape[1]
        head_count = feature_width // DH
        cycle_reach = max(devices // 8, 2)
        cycle_index = lax.axis_index(CTX)
        score_scale = 1.0 / math.sqrt(DH)
        local_pos = jnp.arange(tok_rows, dtype=jnp.int32)
        own_pos = cycle_index * tok_rows + local_pos
        own_docs = doc_ids + 1
        query_heads = query.reshape(tok_rows, head_count, DH)

        grad_full = lax.all_gather(grad_out, FS, axis=1, tiled=True)
        key_value = jnp.concatenate([key, value], axis=1)
        doc_row = jnp.zeros((1, 2 * feature_width), jnp.bfloat16)
        doc_row = doc_row.at[0, :tok_rows].set(own_docs.astype(jnp.bfloat16))
        key_value = jnp.concatenate([key_value, doc_row], axis=0)
        blocks = [(key, value, own_docs)]
        for cycle_step in range(1, cycle_reach + 1):
            got = shifted_by(key_value, devices, cycle_step)
            got_docs = got[tok_rows, :tok_rows].astype(jnp.int32)
            got = got[:tok_rows]
            blocks.append((got[:, :feature_width], got[:, feature_width:], got_docs))

        def scores_of(query_block, key_block):
            return (
                jnp.einsum("tnd,snd->nts", query_block, key_block, preferred_element_type=jnp.float32)
                * score_scale
            )

        state = (
            jnp.full((head_count, tok_rows), NEGATIVE, jnp.float32),
            jnp.zeros((head_count, tok_rows), jnp.float32),
            jnp.zeros((head_count, tok_rows, DH), jnp.float32),
        )
        stored_blocks = []
        for cycle_step in range(cycle_reach + 1):
            key_rows, value_rows, key_docs = blocks[cycle_step]
            key_block = key_rows.reshape(tok_rows, head_count, DH)
            value_block = value_rows.reshape(tok_rows, head_count, DH)
            key_pos = own_pos - cycle_step * tok_rows
            pair_mask = (own_docs[:, None] == key_docs[None, :]) & (
                key_pos[None, :] <= own_pos[:, None]
            )
            forward_row_max, forward_row_sum, forward_output_sum = state
            forward_scores = jnp.where(pair_mask[None], scores_of(query_heads, key_block), NEGATIVE)
            new_max = jnp.maximum(forward_row_max, jnp.max(forward_scores, axis=-1))
            decay_factor = jnp.exp(forward_row_max - new_max)
            forward_weights = jnp.where(
                pair_mask[None], jnp.exp(forward_scores - new_max[..., None]), 0.0
            )
            new_sum = forward_row_sum * decay_factor + jnp.sum(forward_weights, axis=-1)
            weights_low = forward_weights.astype(jnp.bfloat16)
            new_output = forward_output_sum * decay_factor[..., None] + jnp.einsum(
                "nts,snd->ntd", weights_low, value_block, preferred_element_type=jnp.float32
            )
            state = (new_max, new_sum, new_output)
            stored_blocks.append((key_block, value_block, pair_mask))
        row_max, row_sum, output_sum = state
        log_total = row_max + jnp.log(row_sum)
        attn_heads = (output_sum / row_sum[..., None]).astype(jnp.bfloat16).transpose(1, 0, 2)
        attention = attn_heads.reshape(tok_rows, feature_width)

        partial_weight = lax.dot_general(
            attention, grad_full, (((0,), (0,)), ((), ())), preferred_element_type=jnp.float32
        )
        rows_each = partial_weight.shape[0] // devices
        partial_weight = (
            partial_weight.reshape(*CTX_SPLIT, rows_each, partial_weight.shape[1])
            .transpose(1, 2, 0, 3, 4)
            .reshape(partial_weight.shape)
        )
        weight_local, partial_weight = lax.optimization_barrier((out_weight, partial_weight))
        partial_weight = lax.psum_scatter(partial_weight, "cz", scatter_dimension=0, tiled=True)
        weight_rows = gathered_rows(weight_local, cycle_index, devices)
        partial_weight, weight_rows = lax.optimization_barrier((partial_weight, weight_rows))
        grad_weight = lax.psum_scatter(partial_weight, ("cx", "cy"), scatter_dimension=0, tiled=True)

        grad_attn = lax.dot_general(
            grad_full,
            weight_rows,
            (((1,), (1,)), ((), ())),
            preferred_element_type=jnp.float32,
        ).astype(jnp.bfloat16)
        grad_heads = grad_attn.reshape(tok_rows, head_count, DH)
        delta_sum = jnp.einsum(
            "tnd,tnd->nt", grad_heads, attn_heads, preferred_element_type=jnp.float32
        )
        grad_query = jnp.zeros((tok_rows, head_count, DH), jnp.float32)
        grad_key = grad_value = None
        for cycle_step in range(cycle_reach + 1):
            key_block, value_block, pair_mask = stored_blocks[cycle_step]
            scores = scores_of(query_heads, key_block)
            weights = jnp.where(pair_mask[None], jnp.exp(scores - log_total[..., None]), 0.0)
            rounded = weights.astype(jnp.bfloat16)
            value_part = jnp.einsum(
                "nts,tnd->snd", rounded, grad_heads, preferred_element_type=jnp.float32
            )
            grad_weights = jnp.einsum(
                "tnd,snd->nts", grad_heads, value_block, preferred_element_type=jnp.float32
            )
            grad_scores = (weights * (grad_weights - delta_sum[..., None])).astype(jnp.bfloat16)
            query_part = (
                jnp.einsum("nts,snd->tnd", grad_scores, key_block, preferred_element_type=jnp.float32)
                * score_scale
            )
            key_part = (
                jnp.einsum("nts,tnd->snd", grad_scores, query_heads, preferred_element_type=jnp.float32)
                * score_scale
            )
            grad_query = grad_query + query_part
            key_part = key_part.reshape(tok_rows, feature_width)
            value_part = value_part.reshape(tok_rows, feature_width)
            if cycle_step == 0:
                grad_key, grad_value = key_part, value_part
            else:
                sent = jnp.concatenate([key_part, value_part], axis=1).astype(jnp.bfloat16)
                back = shifted_by(sent, devices, -cycle_step).astype(jnp.float32)
                grad_key = grad_key + back[:, :feature_width]
                grad_value = grad_value + back[:, feature_width:]
        return (
            grad_query.reshape(tok_rows, feature_width).astype(jnp.bfloat16),
            grad_key.astype(jnp.bfloat16),
            grad_value.astype(jnp.bfloat16),
            grad_weight,
        )

    return shards


def solution(mesh):
    devices = mesh.shape["ctx"]
    fine = Mesh(mesh.devices.reshape(*CTX_SPLIT, 2, mesh.shape["fsdp"] // 2), CTX + FS)
    return jax.shard_map(
        make_shards(devices),
        mesh=fine,
        in_specs=(
            P(CTX, FS),
            P(CTX, FS),
            P(CTX, FS),
            P(CTX),
            P(FS + CTX, None),
            P(CTX, FS),
        ),
        out_specs=(P(CTX, FS), P(CTX, FS), P(CTX, FS), P(FS + CTX, None)),
        check_vma=False,
    )
```

```python
import math

import jax
import jax.numpy as jnp
from jax import lax
from jax.sharding import Mesh
from jax.sharding import PartitionSpec as P

DH = 128


NEGATIVE = -1e30

CTX = ("cy", "cz", "cx")
FS = ("fy", "fc")
CTX_SPLIT = (2, 8, 4)


def shifted_by(array, devices, by):
    pairs = [(i, i + by) for i in range(devices) if 0 <= i + by < devices]
    return lax.ppermute(array, CTX, pairs)


def exchanged(block, index, devices, bits):
    for bit in bits:
        other = lax.ppermute(block, CTX, [(i, i ^ bit) for i in range(devices)])
        low = (index & bit) == 0
        block = jnp.where(low, jnp.concatenate([block, other]), jnp.concatenate([other, block]))
    return block


def in_device_order(block, bits, rows):
    order = sorted(range(len(bits)), key=lambda k: -bits[k])
    block = block.reshape([2] * len(bits) + list(rows.shape))
    block = block.transpose([len(bits) - 1 - k for k in order] + [len(bits), len(bits) + 1])
    return block.reshape(-1, rows.shape[1])


def make_shards(devices):
    def shards(query, key, value, doc_ids, out_weight, grad_out):
        tok_rows = query.shape[0]
        feature_width = query.shape[1]
        head_count = feature_width // DH
        cycle_reach = max(devices // 8, 2)
        cycle_index = lax.axis_index(CTX)
        score_scale = 1.0 / math.sqrt(DH)
        local_pos = jnp.arange(tok_rows, dtype=jnp.int32)
        own_pos = cycle_index * tok_rows + local_pos
        own_docs = doc_ids + 1
        query_heads = query.reshape(tok_rows, head_count, DH)

        grad_full = lax.all_gather(grad_out, FS, axis=1, tiled=True)
        key_value = jnp.concatenate([key, value], axis=1)
        doc_row = jnp.zeros((1, 2 * feature_width), jnp.bfloat16)
        doc_row = doc_row.at[0, :tok_rows].set(own_docs.astype(jnp.bfloat16))
        key_value = jnp.concatenate([key_value, doc_row], axis=0)
        blocks = [(key, value, own_docs)]
        for cycle_step in range(1, cycle_reach + 1):
            got = shifted_by(key_value, devices, cycle_step)
            got_docs = got[tok_rows, :tok_rows].astype(jnp.int32)
            got = got[:tok_rows]
            blocks.append((got[:, :feature_width], got[:, feature_width:], got_docs))

        def scores_of(query_block, key_block):
            return (
                jnp.einsum("tnd,snd->nts", query_block, key_block, preferred_element_type=jnp.float32)
                * score_scale
            )

        state = (
            jnp.full((head_count, tok_rows), NEGATIVE, jnp.float32),
            jnp.zeros((head_count, tok_rows), jnp.float32),
            jnp.zeros((head_count, tok_rows, DH), jnp.float32),
        )
        stored_blocks = []
        for cycle_step in range(cycle_reach + 1):
            key_rows, value_rows, key_docs = blocks[cycle_step]
            key_block = key_rows.reshape(tok_rows, head_count, DH)
            value_block = value_rows.reshape(tok_rows, head_count, DH)
            key_pos = own_pos - cycle_step * tok_rows
            pair_mask = (own_docs[:, None] == key_docs[None, :]) & (
                key_pos[None, :] <= own_pos[:, None]
            )
            forward_row_max, forward_row_sum, forward_output_sum = state
            forward_scores = jnp.where(pair_mask[None], scores_of(query_heads, key_block), NEGATIVE)
            new_max = jnp.maximum(forward_row_max, jnp.max(forward_scores, axis=-1))
            decay_factor = jnp.exp(forward_row_max - new_max)
            forward_weights = jnp.where(
                pair_mask[None], jnp.exp(forward_scores - new_max[..., None]), 0.0
            )
            new_sum = forward_row_sum * decay_factor + jnp.sum(forward_weights, axis=-1)
            weights_low = forward_weights.astype(jnp.bfloat16)
            new_output = forward_output_sum * decay_factor[..., None] + jnp.einsum(
                "nts,snd->ntd", weights_low, value_block, preferred_element_type=jnp.float32
            )
            state = (new_max, new_sum, new_output)
            stored_blocks.append((key_block, value_block, pair_mask))
        row_max, row_sum, output_sum = state
        log_total = row_max + jnp.log(row_sum)
        attn_heads = (output_sum / row_sum[..., None]).astype(jnp.bfloat16).transpose(1, 0, 2)
        attention = attn_heads.reshape(tok_rows, feature_width)

        partial_weight = lax.dot_general(
            attention, grad_full, (((0,), (0,)), ((), ())), preferred_element_type=jnp.float32
        )
        rows_each = partial_weight.shape[0] // devices
        partial_weight = (
            partial_weight.reshape(*CTX_SPLIT, rows_each, partial_weight.shape[1])
            .transpose(1, 2, 0, 3, 4)
            .reshape(partial_weight.shape)
        )
        early_bits = [devices >> k for k in (2, 3, 4) if devices >> k >= 1]
        late_bits = [devices >> k for k in (5, 1, 6) if devices >> k >= 1]
        weight_early = exchanged(out_weight, cycle_index, devices, early_bits)
        weight_early, partial_weight = lax.optimization_barrier((weight_early, partial_weight))
        partial_weight = lax.psum_scatter(partial_weight, "cz", scatter_dimension=0, tiled=True)
        weight_rows = in_device_order(
            exchanged(weight_early, cycle_index, devices, late_bits), early_bits + late_bits, out_weight
        )
        partial_weight, weight_rows = lax.optimization_barrier((partial_weight, weight_rows))
        grad_weight = lax.psum_scatter(partial_weight, ("cx", "cy"), scatter_dimension=0, tiled=True)

        grad_attn = lax.dot_general(
            grad_full,
            weight_rows,
            (((1,), (1,)), ((), ())),
            preferred_element_type=jnp.float32,
        ).astype(jnp.bfloat16)
        grad_heads = grad_attn.reshape(tok_rows, head_count, DH)
        delta_sum = jnp.einsum(
            "tnd,tnd->nt", grad_heads, attn_heads, preferred_element_type=jnp.float32
        )
        grad_query = jnp.zeros((tok_rows, head_count, DH), jnp.float32)
        grad_key = grad_value = None
        for cycle_step in range(cycle_reach + 1):
            key_block, value_block, pair_mask = stored_blocks[cycle_step]
            scores = scores_of(query_heads, key_block)
            weights = jnp.where(pair_mask[None], jnp.exp(scores - log_total[..., None]), 0.0)
            rounded = weights.astype(jnp.bfloat16)
            value_part = jnp.einsum(
                "nts,tnd->snd", rounded, grad_heads, preferred_element_type=jnp.float32
            )
            grad_weights = jnp.einsum(
                "tnd,snd->nts", grad_heads, value_block, preferred_element_type=jnp.float32
            )
            grad_scores = (weights * (grad_weights - delta_sum[..., None])).astype(jnp.bfloat16)
            query_part = (
                jnp.einsum("nts,snd->tnd", grad_scores, key_block, preferred_element_type=jnp.float32)
                * score_scale
            )
            key_part = (
                jnp.einsum("nts,tnd->snd", grad_scores, query_heads, preferred_element_type=jnp.float32)
                * score_scale
            )
            grad_query = grad_query + query_part
            key_part = key_part.reshape(tok_rows, feature_width)
            value_part = value_part.reshape(tok_rows, feature_width)
            if cycle_step == 0:
                grad_key, grad_value = key_part, value_part
            else:
                sent = jnp.concatenate([key_part, value_part], axis=1).astype(jnp.bfloat16)
                back = shifted_by(sent, devices, -cycle_step).astype(jnp.float32)
                grad_key = grad_key + back[:, :feature_width]
                grad_value = grad_value + back[:, feature_width:]
        return (
            grad_query.reshape(tok_rows, feature_width).astype(jnp.bfloat16),
            grad_key.astype(jnp.bfloat16),
            grad_value.astype(jnp.bfloat16),
            grad_weight,
        )

    return shards


def solution(mesh):
    devices = mesh.shape["ctx"]
    fine = Mesh(mesh.devices.reshape(*CTX_SPLIT, 2, mesh.shape["fsdp"] // 2), CTX + FS)
    return jax.shard_map(
        make_shards(devices),
        mesh=fine,
        in_specs=(
            P(CTX, FS),
            P(CTX, FS),
            P(CTX, FS),
            P(CTX),
            P(FS + CTX, None),
            P(CTX, FS),
        ),
        out_specs=(P(CTX, FS), P(CTX, FS), P(CTX, FS), P(FS + CTX, None)),
        check_vma=False,
    )
```

```python
import math

import jax
import jax.numpy as jnp
from jax import lax
from jax.sharding import Mesh
from jax.sharding import PartitionSpec as P

DH = 128


NEGATIVE = -1e30

CTX = ("cy", "cz", "cx")
FS = ("fy", "fc")
CTX_SPLIT = (2, 8, 4)


def shifted_by(array, devices, by):
    pairs = [(i, i + by) for i in range(devices) if 0 <= i + by < devices]
    return lax.ppermute(array, CTX, pairs)


def exchanged(block, index, devices, bits):
    for bit in bits:
        other = lax.ppermute(block, CTX, [(i, i ^ bit) for i in range(devices)])
        low = (index & bit) == 0
        block = jnp.where(low, jnp.concatenate([block, other]), jnp.concatenate([other, block]))
    return block


def in_device_order(block, bits, rows):
    order = sorted(range(len(bits)), key=lambda k: -bits[k])
    block = block.reshape([2] * len(bits) + list(rows.shape))
    block = block.transpose([len(bits) - 1 - k for k in order] + [len(bits), len(bits) + 1])
    return block.reshape(-1, rows.shape[1])


def spread_rows(block, index, devices, early_bits, late_bits, rows):
    def device_mask(m):
        return sum(bit for k, bit in enumerate(late_bits) if (m >> k) & 1)

    own = sum(((index & bit) != 0).astype(jnp.int32) << k for k, bit in enumerate(late_bits))
    parts = [block]
    for m in range(1, 1 << len(late_bits)):
        mask = device_mask(m)
        parts.append(lax.ppermute(block, CTX, [(i, i ^ mask) for i in range(devices)]))
    stacked = jnp.stack(parts)
    stacked = jnp.take(stacked, jnp.arange(1 << len(late_bits), dtype=jnp.int32) ^ own, axis=0)
    bits = list(reversed(late_bits)) + list(reversed(early_bits))
    stacked = stacked.reshape([2] * len(bits) + list(rows.shape))
    order = sorted(range(len(bits)), key=lambda k: -bits[k])
    stacked = stacked.transpose(order + [len(bits), len(bits) + 1])
    return stacked.reshape(-1, rows.shape[1])


def make_shards(devices):
    def shards(query, key, value, doc_ids, out_weight, grad_out):
        tok_rows = query.shape[0]
        feature_width = query.shape[1]
        head_count = feature_width // DH
        cycle_reach = max(devices // 8, 2)
        cycle_index = lax.axis_index(CTX)
        score_scale = 1.0 / math.sqrt(DH)
        local_pos = jnp.arange(tok_rows, dtype=jnp.int32)
        own_pos = cycle_index * tok_rows + local_pos
        own_docs = doc_ids + 1
        query_heads = query.reshape(tok_rows, head_count, DH)

        grad_full = lax.all_gather(grad_out, FS, axis=1, tiled=True)
        key_value = jnp.concatenate([key, value], axis=1)
        doc_row = jnp.zeros((1, 2 * feature_width), jnp.bfloat16)
        doc_row = doc_row.at[0, :tok_rows].set(own_docs.astype(jnp.bfloat16))
        key_value = jnp.concatenate([key_value, doc_row], axis=0)
        blocks = [(key, value, own_docs)]
        for cycle_step in range(1, cycle_reach + 1):
            got = shifted_by(key_value, devices, cycle_step)
            got_docs = got[tok_rows, :tok_rows].astype(jnp.int32)
            got = got[:tok_rows]
            blocks.append((got[:, :feature_width], got[:, feature_width:], got_docs))

        def scores_of(query_block, key_block):
            return (
                jnp.einsum("tnd,snd->nts", query_block, key_block, preferred_element_type=jnp.float32)
                * score_scale
            )

        state = (
            jnp.full((head_count, tok_rows), NEGATIVE, jnp.float32),
            jnp.zeros((head_count, tok_rows), jnp.float32),
            jnp.zeros((head_count, tok_rows, DH), jnp.float32),
        )
        stored_blocks = []
        for cycle_step in range(cycle_reach + 1):
            key_rows, value_rows, key_docs = blocks[cycle_step]
            key_block = key_rows.reshape(tok_rows, head_count, DH)
            value_block = value_rows.reshape(tok_rows, head_count, DH)
            key_pos = own_pos - cycle_step * tok_rows
            pair_mask = (own_docs[:, None] == key_docs[None, :]) & (
                key_pos[None, :] <= own_pos[:, None]
            )
            forward_row_max, forward_row_sum, forward_output_sum = state
            forward_scores = jnp.where(pair_mask[None], scores_of(query_heads, key_block), NEGATIVE)
            new_max = jnp.maximum(forward_row_max, jnp.max(forward_scores, axis=-1))
            decay_factor = jnp.exp(forward_row_max - new_max)
            forward_weights = jnp.where(
                pair_mask[None], jnp.exp(forward_scores - new_max[..., None]), 0.0
            )
            new_sum = forward_row_sum * decay_factor + jnp.sum(forward_weights, axis=-1)
            weights_low = forward_weights.astype(jnp.bfloat16)
            new_output = forward_output_sum * decay_factor[..., None] + jnp.einsum(
                "nts,snd->ntd", weights_low, value_block, preferred_element_type=jnp.float32
            )
            state = (new_max, new_sum, new_output)
            stored_blocks.append((key_block, value_block, pair_mask))
        row_max, row_sum, output_sum = state
        log_total = row_max + jnp.log(row_sum)
        attn_heads = (output_sum / row_sum[..., None]).astype(jnp.bfloat16).transpose(1, 0, 2)
        attention = attn_heads.reshape(tok_rows, feature_width)

        partial_weight = lax.dot_general(
            attention, grad_full, (((0,), (0,)), ((), ())), preferred_element_type=jnp.float32
        )
        rows_each = partial_weight.shape[0] // devices
        partial_weight = (
            partial_weight.reshape(*CTX_SPLIT, rows_each, partial_weight.shape[1])
            .transpose(1, 2, 0, 3, 4)
            .reshape(partial_weight.shape)
        )
        early_bits = [devices >> k for k in (2, 3, 4) if devices >> k >= 1]
        late_bits = [devices >> k for k in (6, 5, 1) if devices >> k >= 1]
        weight_early = exchanged(out_weight, cycle_index, devices, early_bits)
        weight_early, partial_weight = lax.optimization_barrier((weight_early, partial_weight))
        partial_weight = lax.psum_scatter(partial_weight, "cz", scatter_dimension=0, tiled=True)
        weight_rows = spread_rows(weight_early, cycle_index, devices, early_bits, late_bits, out_weight)
        partial_weight, weight_rows = lax.optimization_barrier((partial_weight, weight_rows))
        grad_weight = lax.psum_scatter(partial_weight, ("cx", "cy"), scatter_dimension=0, tiled=True)

        grad_attn = lax.dot_general(
            grad_full,
            weight_rows,
            (((1,), (1,)), ((), ())),
            preferred_element_type=jnp.float32,
        ).astype(jnp.bfloat16)
        grad_heads = grad_attn.reshape(tok_rows, head_count, DH)
        delta_sum = jnp.einsum(
            "tnd,tnd->nt", grad_heads, attn_heads, preferred_element_type=jnp.float32
        )
        grad_query = jnp.zeros((tok_rows, head_count, DH), jnp.float32)
        grad_key = grad_value = None
        for cycle_step in range(cycle_reach + 1):
            key_block, value_block, pair_mask = stored_blocks[cycle_step]
            scores = scores_of(query_heads, key_block)
            weights = jnp.where(pair_mask[None], jnp.exp(scores - log_total[..., None]), 0.0)
            rounded = weights.astype(jnp.bfloat16)
            value_part = jnp.einsum(
                "nts,tnd->snd", rounded, grad_heads, preferred_element_type=jnp.float32
            )
            grad_weights = jnp.einsum(
                "tnd,snd->nts", grad_heads, value_block, preferred_element_type=jnp.float32
            )
            grad_scores = (weights * (grad_weights - delta_sum[..., None])).astype(jnp.bfloat16)
            query_part = (
                jnp.einsum("nts,snd->tnd", grad_scores, key_block, preferred_element_type=jnp.float32)
                * score_scale
            )
            key_part = (
                jnp.einsum("nts,tnd->snd", grad_scores, query_heads, preferred_element_type=jnp.float32)
                * score_scale
            )
            grad_query = grad_query + query_part
            key_part = key_part.reshape(tok_rows, feature_width)
            value_part = value_part.reshape(tok_rows, feature_width)
            if cycle_step == 0:
                grad_key, grad_value = key_part, value_part
            else:
                sent = jnp.concatenate([key_part, value_part], axis=1).astype(jnp.bfloat16)
                back = shifted_by(sent, devices, -cycle_step).astype(jnp.float32)
                grad_key = grad_key + back[:, :feature_width]
                grad_value = grad_value + back[:, feature_width:]
        return (
            grad_query.reshape(tok_rows, feature_width).astype(jnp.bfloat16),
            grad_key.astype(jnp.bfloat16),
            grad_value.astype(jnp.bfloat16),
            grad_weight,
        )

    return shards


def solution(mesh):
    devices = mesh.shape["ctx"]
    fine = Mesh(mesh.devices.reshape(*CTX_SPLIT, 2, mesh.shape["fsdp"] // 2), CTX + FS)
    return jax.shard_map(
        make_shards(devices),
        mesh=fine,
        in_specs=(
            P(CTX, FS),
            P(CTX, FS),
            P(CTX, FS),
            P(CTX),
            P(FS + CTX, None),
            P(CTX, FS),
        ),
        out_specs=(P(CTX, FS), P(CTX, FS), P(CTX, FS), P(FS + CTX, None)),
        check_vma=False,
    )
```

```python
import math

import jax
import jax.numpy as jnp
from jax import lax
from jax.sharding import Mesh
from jax.sharding import PartitionSpec as P

DH = 128


NEGATIVE = -1e30

CTX = ("cy", "cz", "cx")
FS = ("fy", "fc")
CTX_SPLIT = (2, 8, 4)


def shifted_by(array, devices, by):
    pairs = [(i, i + by) for i in range(devices) if 0 <= i + by < devices]
    return lax.ppermute(array, CTX, pairs)


def exchanged(block, index, devices, bits):
    for bit in bits:
        other = lax.ppermute(block, CTX, [(i, i ^ bit) for i in range(devices)])
        low = (index & bit) == 0
        block = jnp.where(low, jnp.concatenate([block, other]), jnp.concatenate([other, block]))
    return block


def in_device_order(block, bits, rows):
    order = sorted(range(len(bits)), key=lambda k: -bits[k])
    block = block.reshape([2] * len(bits) + list(rows.shape))
    block = block.transpose([len(bits) - 1 - k for k in order] + [len(bits), len(bits) + 1])
    return block.reshape(-1, rows.shape[1])


def make_shards(devices):
    def shards(query, key, value, doc_ids, out_weight, grad_out):
        tok_rows = query.shape[0]
        feature_width = query.shape[1]
        head_count = feature_width // DH
        cycle_reach = max(devices // 8, 2)
        cycle_index = lax.axis_index(CTX)
        score_scale = 1.0 / math.sqrt(DH)
        local_pos = jnp.arange(tok_rows, dtype=jnp.int32)
        own_pos = cycle_index * tok_rows + local_pos
        own_docs = doc_ids + 1
        query_heads = query.reshape(tok_rows, head_count, DH)

        grad_full = lax.all_gather(grad_out, FS, axis=1, tiled=True)
        key_value = jnp.concatenate([key, value], axis=1)
        doc_row = jnp.zeros((1, 2 * feature_width), jnp.bfloat16)
        doc_row = doc_row.at[0, :tok_rows].set(own_docs.astype(jnp.bfloat16))
        key_value = jnp.concatenate([key_value, doc_row], axis=0)
        blocks = [(key, value, own_docs)]
        for cycle_step in range(1, cycle_reach + 1):
            got = shifted_by(key_value, devices, cycle_step)
            got_docs = got[tok_rows, :tok_rows].astype(jnp.int32)
            got = got[:tok_rows]
            blocks.append((got[:, :feature_width], got[:, feature_width:], got_docs))

        def scores_of(query_block, key_block):
            return (
                jnp.einsum("tnd,snd->nts", query_block, key_block, preferred_element_type=jnp.float32)
                * score_scale
            )

        state = (
            jnp.full((head_count, tok_rows), NEGATIVE, jnp.float32),
            jnp.zeros((head_count, tok_rows), jnp.float32),
            jnp.zeros((head_count, tok_rows, DH), jnp.float32),
        )
        stored_blocks = []
        for cycle_step in range(cycle_reach + 1):
            key_rows, value_rows, key_docs = blocks[cycle_step]
            key_block = key_rows.reshape(tok_rows, head_count, DH)
            value_block = value_rows.reshape(tok_rows, head_count, DH)
            key_pos = own_pos - cycle_step * tok_rows
            pair_mask = (own_docs[:, None] == key_docs[None, :]) & (
                key_pos[None, :] <= own_pos[:, None]
            )
            forward_row_max, forward_row_sum, forward_output_sum = state
            forward_scores = jnp.where(pair_mask[None], scores_of(query_heads, key_block), NEGATIVE)
            new_max = jnp.maximum(forward_row_max, jnp.max(forward_scores, axis=-1))
            decay_factor = jnp.exp(forward_row_max - new_max)
            forward_weights = jnp.where(
                pair_mask[None], jnp.exp(forward_scores - new_max[..., None]), 0.0
            )
            new_sum = forward_row_sum * decay_factor + jnp.sum(forward_weights, axis=-1)
            weights_low = forward_weights.astype(jnp.bfloat16)
            new_output = forward_output_sum * decay_factor[..., None] + jnp.einsum(
                "nts,snd->ntd", weights_low, value_block, preferred_element_type=jnp.float32
            )
            state = (new_max, new_sum, new_output)
            stored_blocks.append((key_block, value_block, pair_mask))
        row_max, row_sum, output_sum = state
        log_total = row_max + jnp.log(row_sum)
        attn_heads = (output_sum / row_sum[..., None]).astype(jnp.bfloat16).transpose(1, 0, 2)
        attention = attn_heads.reshape(tok_rows, feature_width)

        partial_weight = lax.dot_general(
            attention, grad_full, (((0,), (0,)), ((), ())), preferred_element_type=jnp.float32
        )
        rows_each = partial_weight.shape[0] // devices
        partial_weight = (
            partial_weight.reshape(*CTX_SPLIT, rows_each, partial_weight.shape[1])
            .transpose(1, 2, 0, 3, 4)
            .reshape(partial_weight.shape)
        )
        early_bits = [devices >> k for k in (2, 3, 4, 5) if devices >> k >= 1]
        late_bits = [devices >> k for k in (1, 6) if devices >> k >= 1]
        weight_early = exchanged(out_weight, cycle_index, devices, early_bits)
        weight_early, partial_weight = lax.optimization_barrier((weight_early, partial_weight))
        partial_weight = lax.psum_scatter(partial_weight, "cz", scatter_dimension=0, tiled=True)
        weight_rows = in_device_order(
            exchanged(weight_early, cycle_index, devices, late_bits), early_bits + late_bits, out_weight
        )
        partial_weight, weight_rows = lax.optimization_barrier((partial_weight, weight_rows))
        grad_weight = lax.psum_scatter(partial_weight, ("cx", "cy"), scatter_dimension=0, tiled=True)

        grad_attn = lax.dot_general(
            grad_full,
            weight_rows,
            (((1,), (1,)), ((), ())),
            preferred_element_type=jnp.float32,
        ).astype(jnp.bfloat16)
        grad_heads = grad_attn.reshape(tok_rows, head_count, DH)
        delta_sum = jnp.einsum(
            "tnd,tnd->nt", grad_heads, attn_heads, preferred_element_type=jnp.float32
        )
        grad_query = jnp.zeros((tok_rows, head_count, DH), jnp.float32)
        grad_key = grad_value = None
        for cycle_step in range(cycle_reach + 1):
            key_block, value_block, pair_mask = stored_blocks[cycle_step]
            scores = scores_of(query_heads, key_block)
            weights = jnp.where(pair_mask[None], jnp.exp(scores - log_total[..., None]), 0.0)
            rounded = weights.astype(jnp.bfloat16)
            value_part = jnp.einsum(
                "nts,tnd->snd", rounded, grad_heads, preferred_element_type=jnp.float32
            )
            grad_weights = jnp.einsum(
                "tnd,snd->nts", grad_heads, value_block, preferred_element_type=jnp.float32
            )
            grad_scores = (weights * (grad_weights - delta_sum[..., None])).astype(jnp.bfloat16)
            query_part = (
                jnp.einsum("nts,snd->tnd", grad_scores, key_block, preferred_element_type=jnp.float32)
                * score_scale
            )
            key_part = (
                jnp.einsum("nts,tnd->snd", grad_scores, query_heads, preferred_element_type=jnp.float32)
                * score_scale
            )
            grad_query = grad_query + query_part
            key_part = key_part.reshape(tok_rows, feature_width)
            value_part = value_part.reshape(tok_rows, feature_width)
            if cycle_step == 0:
                grad_key, grad_value = key_part, value_part
            else:
                sent = jnp.concatenate([key_part, value_part], axis=1).astype(jnp.bfloat16)
                back = shifted_by(sent, devices, -cycle_step).astype(jnp.float32)
                grad_key = grad_key + back[:, :feature_width]
                grad_value = grad_value + back[:, feature_width:]
        return (
            grad_query.reshape(tok_rows, feature_width).astype(jnp.bfloat16),
            grad_key.astype(jnp.bfloat16),
            grad_value.astype(jnp.bfloat16),
            grad_weight,
        )

    return shards


def solution(mesh):
    devices = mesh.shape["ctx"]
    fine = Mesh(mesh.devices.reshape(*CTX_SPLIT, 2, mesh.shape["fsdp"] // 2), CTX + FS)
    return jax.shard_map(
        make_shards(devices),
        mesh=fine,
        in_specs=(
            P(CTX, FS),
            P(CTX, FS),
            P(CTX, FS),
            P(CTX),
            P(FS + CTX, None),
            P(CTX, FS),
        ),
        out_specs=(P(CTX, FS), P(CTX, FS), P(CTX, FS), P(FS + CTX, None)),
        check_vma=False,
    )
```
